128 devices in a mesh: depth: 8 (over z, core), plane: 16 (over x, y).
Axes of the slice: x: 4, y: 4, z: 4, core: 2. Of those that a mesh axis runs over, the one named last changes fastest.
Arguments:
- toar: bfloat16 [8, 8, 2, 32768], P('depth', None, None, 'plane'), may hold values from -6 to 6
- pml_coeff: float32 [8, 2, 32768], P('depth', None, 'plane'), may hold values from -1.5 to 1.5
- coupling: float32 [8, 32768], P('depth', 'plane'), may hold values from 0.5 to 1
- inverse: bfloat16 [8, 512, 16, 64, 128], P('depth', 'plane'), may hold values from -0.125 to 0.125
- pattern: int32 [8, 512, 16], P('depth', 'plane'), may hold values from 0 to 511
- patch_map: int32 [8, 32768], P('depth', 'plane'), may hold values from 0 to 16383, as said below
Outputs:
- precond: bfloat16 [8, 8, 2, 32768], P('depth', None, None, 'plane')
- patch_sens: float32 [8, 16384], P(None, ('depth', 'plane'))
The draws below stay inside these ranges and needn't reach their ends.
Inputs may be any that keep to these rules, and one draw needn't show every extreme that they name: `patch_map`: patch p belongs to owner p // 128. Among the cells of one device (one layer, one block of 2048 cells), at most 32 name patches of any one owner, and in every such block some owner is named exactly 32 times. `pattern`: block columns of the whole layer.
All inputs are finite; a program needn't handle non-finite values.
Results may differ from the reference program's by a relative error of at most 0.018.
Values may be sent and summed in bfloat16 or wider, within the bound.
No kernel may reach another device: no remote copies, remote signals or barrier semaphores. Data moves between devices by JAX's collectives and lax.ppermute only.
A program may use at most 128 MiB of HBM per device.

```python
import math
import jax
import jax.numpy as jnp

BLK = 64
KNZ = 16
NV = 8
NB_DEV = 32
PATCH_DEV = 128
LAYERS = 8
NBLK = 512
CELLS = 32768
OWNERS = 128
PATCHES = 16384
CAP = 32


def block_owners(key):
    rows = NB_DEV * BLK
    total = OWNERS * CAP
    key_a, key_b, key_c, key_d = jax.random.split(key, 4)
    owner_list = jnp.arange(total, dtype=jnp.int32) // CAP
    favored = jax.random.randint(key_a, (), 0, OWNERS, dtype=jnp.int32)
    priority = jax.random.permutation(key_b, total).astype(jnp.int32)
    priority = jnp.where(owner_list == favored, priority - total, priority)
    order = jnp.argsort(priority, stable=True)
    picked = owner_list[order[:rows]]
    shuffled = picked[jax.random.permutation(key_c, rows)]
    local = jax.random.randint(key_d, (rows,), 0, PATCH_DEV, dtype=jnp.int32)
    return shuffled * PATCH_DEV + local


def draw_patch_map(key, part):
    keys = jax.random.split(jax.random.fold_in(key, 7), OWNERS)
    maps = jax.vmap(block_owners)(keys)
    return maps.reshape(LAYERS, CELLS).astype(jnp.int32)


def set_ends(entries, rng, low, largest):
    longest = entries.shape.index(max(entries.shape))
    spots = []
    for shift in (0, 1):
        where = [jax.random.randint(jax.random.fold_in(rng, axis), (), 0, length) for axis, length in enumerate(entries.shape)]
        where[longest] = (where[longest] + shift) % entries.shape[longest]
        spots.append(tuple(where))
    return entries.at[spots[0]].set(low).at[spots[1]].set(largest)


def level_of(own_key, dims, cuts, least, largest):
    gain, own = 1.0, jax.random.fold_in(own_key, 6)
    for position, blocks in cuts:
        draws = jnp.exp(jax.random.uniform(jax.random.fold_in(own, position), (blocks,), jnp.float32, least / len(cuts), largest / len(cuts)))
        gain = gain * jnp.repeat(draws, dims[position] // blocks).reshape([-1 if axis == position else 1 for axis in range(len(dims))])
    return gain


def scatter_about(key, extent, scale, limit, pieces=(), kind=jnp.bfloat16):
    loudness = level_of(key, extent, pieces, -0.22, 0.18) if pieces else 1.0
    array = jax.random.normal(key, extent, jnp.float32) * scale * loudness
    return jnp.minimum(jnp.maximum(array, -limit), limit).astype(kind)


def setup_inputs(seed: int = 0) -> dict:
    key_list = jax.random.split(jax.random.key(seed), 7)
    return {
        "toar": scatter_about(key_list[0], (LAYERS, NV, 2, CELLS), 1.0, 6.0, ((0, 8), (3, 16))),
        "pml_coeff": jnp.clip(jax.random.uniform(key_list[1], (LAYERS, 2, CELLS), jnp.float32, -1.5, 1.5) * level_of(key_list[1], (LAYERS, 2, CELLS), ((0, 8), (2, 16)), -0.4, 0.0), -1.5, 1.5),
        "coupling": jnp.clip(jnp.exp(math.log(1.0) - 0.6931472 * jax.random.uniform(key_list[2], (LAYERS, CELLS), jnp.float32) ** level_of(key_list[2], (LAYERS, CELLS), ((0, 8), (1, 16)), -0.2, 0.2)), 0.5, 1.0),
        "inverse": scatter_about(key_list[3], (LAYERS, NBLK, KNZ, BLK, 2 * BLK), (2 * KNZ * BLK) ** -0.5, 0.125, ((0, 8), (1, 16))),
        "pattern": set_ends(jax.random.randint(key_list[4], (LAYERS, NBLK, KNZ), 0, NBLK), jax.random.fold_in(key_list[4], 1), 0, NBLK - 1).astype(jnp.int32),
        "patch_map": draw_patch_map(jax.random.fold_in(key_list[6], 71), 0),
    }


def apply_layer(vectors, inv_layer, pattern_layer):
    count = vectors.shape[0]
    block_rows = inv_layer.shape[0]
    per_row = inv_layer.shape[1]
    block_cells = inv_layer.shape[2]
    blocks = vectors.astype(jnp.float32).reshape(count, 2, block_rows, block_cells)
    chosen = jnp.take(blocks, pattern_layer.reshape(-1).astype(jnp.int32), axis=2)
    chosen = chosen.reshape(count, 2, block_rows, per_row, block_cells)
    factor = inv_layer.astype(jnp.float32).reshape(block_rows, per_row, block_cells, 2, block_cells)
    partial_value = jnp.einsum('rkiaj,vbrkj->vabri', factor, chosen)
    real_part = partial_value[:, 0, 0] - partial_value[:, 1, 1]
    imag_part = partial_value[:, 0, 1] + partial_value[:, 1, 0]
    return jnp.stack([real_part, imag_part], axis=1).reshape(count, 2, block_rows * block_cells)


def reference(toar, pml_coeff, coupling, inverse, pattern, patch_map):
    layers = toar.shape[0]
    toar_f32 = toar.astype(jnp.float32)
    sources = []
    for layer in range(layers):
        coeff = pml_coeff[layer]
        real_part = coeff[0] * toar_f32[layer, :, 0] - coeff[1] * toar_f32[layer, :, 1]
        imag_part = coeff[0] * toar_f32[layer, :, 1] + coeff[1] * toar_f32[layer, :, 0]
        sources.append(jnp.stack([real_part, imag_part], axis=1))
    swept = []
    for layer in range(layers):
        down_in = sources[layer]
        if layer > 0:
            down_in = down_in + coupling[layer] * swept[layer - 1].astype(jnp.float32)
        result = apply_layer(down_in.astype(jnp.bfloat16), inverse[layer], pattern[layer])
        swept.append(result.astype(jnp.bfloat16))
    precond = [None] * layers
    precond[layers - 1] = swept[layers - 1]
    for layer in range(layers - 2, -1, -1):
        up_in = (coupling[layer + 1] * precond[layer + 1].astype(jnp.float32)).astype(jnp.bfloat16)
        result = swept[layer].astype(jnp.float32) + apply_layer(up_in, inverse[layer], pattern[layer])
        precond[layer] = result.astype(jnp.bfloat16)
    stacked = jnp.stack(precond, axis=0)
    product = stacked.astype(jnp.float32) * toar_f32
    contrib = product[:, :, 0] + product[:, :, 1]
    contrib = jnp.transpose(contrib, (1, 0, 2)).reshape(contrib.shape[1], -1)
    sums = jax.ops.segment_sum(contrib.T, patch_map.reshape(-1).astype(jnp.int32), num_segments=PATCHES)
    return stacked, sums.T
```

```python
import jax
import jax.numpy as jnp
from jax import lax
from jax.sharding import PartitionSpec as P

PATCH_DEV = 128
CAP = 32


def passed_along(value, axis, steps):
    count = lax.axis_size(axis)
    first, last = (max(0, -steps), min(count, count - steps))
    return lax.ppermute(value, axis, [(source, source + steps) for source in range(first, last)])


def shards(toar, pml_coeff, coupling, inverse, pattern, patch_map):
    toar_local = toar[0]
    coeff = pml_coeff[0]
    coupler = coupling[0]
    factor = inverse[0]
    pattern_flat = pattern[0].reshape(-1)
    block_rows = factor.shape[0]
    block_cells = factor.shape[2]
    depth_count = lax.axis_size("depth")
    plane_count = lax.axis_size("plane")
    vec_count = toar_local.shape[0]
    toar_f32 = toar_local.astype(jnp.float32)
    real_part = coeff[0] * toar_f32[:, 0] - coeff[1] * toar_f32[:, 1]
    imag_part = coeff[0] * toar_f32[:, 1] + coeff[1] * toar_f32[:, 0]
    source = jnp.stack([real_part, imag_part], axis=1)

    def apply_layer(incoming):
        local_blocks = incoming.reshape(vec_count, 2, block_rows, block_cells).transpose(2, 0, 1, 3)
        gathered = lax.all_gather(local_blocks, "plane", axis=0, tiled=True)
        chosen = jnp.take(gathered, pattern_flat, axis=0)
        chosen = chosen.reshape(block_rows, -1, vec_count, 2, block_cells)
        x_re = chosen[:, :, :, 0]
        x_im = chosen[:, :, :, 1]
        expanded = jnp.stack(
            [jnp.concatenate([x_re, -x_im], axis=-1), jnp.concatenate([x_im, x_re], axis=-1)],
            axis=3,
        )
        out = jnp.einsum(
            "rkic,rkvwc->vwri", factor, expanded, preferred_element_type=jnp.float32
        )
        return out.reshape(vec_count, 2, block_rows * block_cells)

    def down_turn(turn_index, current):
        arrived = passed_along(current, "depth", 1)
        down_in = (source + coupler * arrived.astype(jnp.float32)).astype(jnp.bfloat16)
        return apply_layer(down_in).astype(jnp.bfloat16)

    first = apply_layer(source.astype(jnp.bfloat16)).astype(jnp.bfloat16)
    swept = lax.fori_loop(0, depth_count - 1, down_turn, first)

    def up_turn(turn_index, current):
        outgoing = (coupler * current.astype(jnp.float32)).astype(jnp.bfloat16)
        arrived = passed_along(outgoing, "depth", -1)
        return (swept.astype(jnp.float32) + apply_layer(arrived)).astype(jnp.bfloat16)

    precond = lax.fori_loop(0, depth_count - 1, up_turn, swept)
    product = precond.astype(jnp.float32) * toar_f32
    contrib = product[:, 0] + product[:, 1]

    cell_patch = patch_map[0]
    cell_count = cell_patch.shape[0]
    owner_count = depth_count * plane_count
    owner = cell_patch // PATCH_DEV
    hits = (owner[:, None] == jnp.arange(owner_count, dtype=owner.dtype)[None, :]).astype(jnp.int32)
    rank = jnp.take_along_axis(jnp.cumsum(hits, axis=0), owner[:, None], axis=1)[:, 0] - 1
    slot = owner * CAP + rank
    cells = jnp.arange(cell_count, dtype=jnp.int32)
    perm = jnp.full((owner_count * CAP,), cell_count, jnp.int32).at[slot].set(cells)
    local_patch = (cell_patch % PATCH_DEV).astype(jnp.float32)
    padded = jnp.concatenate(
        [jnp.concatenate([contrib.T, local_patch[:, None]], axis=1),
         jnp.zeros((1, vec_count + 1), jnp.float32)],
        axis=0,
    )
    packed = jnp.take(padded, perm, axis=0).reshape(owner_count, CAP, vec_count + 1)
    received = lax.all_to_all(packed, ("depth", "plane"), 0, 0, tiled=True)
    received = received.reshape(owner_count * CAP, vec_count + 1)
    target = received[:, vec_count].astype(jnp.int32)
    owned = jax.ops.segment_sum(received[:, :vec_count], target, num_segments=PATCH_DEV).T
    return (precond[None], owned)


def solution(mesh):
    return jax.shard_map(
        shards,
        mesh=mesh,
        in_specs=(
            P("depth", None, None, "plane"),
            P("depth", None, "plane"),
            P("depth", "plane"),
            P("depth", "plane", None, None, None),
            P("depth", "plane", None),
            P("depth", "plane"),
        ),
        out_specs=(P("depth", None, None, "plane"), P(None, ("depth", "plane"))),
        check_vma=False,
    )
```

```python
import jax
import jax.numpy as jnp
from jax import lax
from jax.sharding import PartitionSpec as P

PATCH_DEV = 128
CAP = 32


def passed_along(value, axis, steps):
    count = lax.axis_size(axis)
    first, last = (max(0, -steps), min(count, count - steps))
    return lax.ppermute(value, axis, [(source, source + steps) for source in range(first, last)])


def shards(toar, pml_coeff, coupling, inverse, pattern, patch_map):
    toar_local = toar[0]
    coeff = pml_coeff[0]
    coupler = coupling[0]
    factor = inverse[0]
    pattern_flat = pattern[0].reshape(-1)
    block_rows = factor.shape[0]
    block_cells = factor.shape[2]
    depth_count = lax.axis_size("depth")
    plane_count = lax.axis_size("plane")
    vec_count = toar_local.shape[0]
    toar_f32 = toar_local.astype(jnp.float32)
    real_part = coeff[0] * toar_f32[:, 0] - coeff[1] * toar_f32[:, 1]
    imag_part = coeff[0] * toar_f32[:, 1] + coeff[1] * toar_f32[:, 0]
    source = jnp.stack([real_part, imag_part], axis=1)

    side_a = next(n for n in range(int(plane_count ** 0.5), 0, -1) if plane_count % n == 0)
    side_b = plane_count // side_a
    plane_routes = {}
    for offset in range(1, plane_count):
        step_a, step_b = divmod(offset, side_b)
        plane_routes[offset] = [
            (a * side_b + b, ((a + step_a) % side_a) * side_b + (b + step_b) % side_b)
            for a in range(side_a)
            for b in range(side_b)
        ]
    here = lax.axis_index("plane")
    origin = pattern_flat // block_rows
    slot_a = (here // side_b - origin // side_b) % side_a
    slot_b = (here % side_b - origin % side_b) % side_b
    remapped = (slot_a * side_b + slot_b) * block_rows + pattern_flat % block_rows

    def apply_layer(incoming):
        local_blocks = incoming.reshape(vec_count, 2, block_rows, block_cells).transpose(2, 0, 1, 3)
        pieces = [local_blocks]
        for offset in range(1, plane_count):
            pieces.append(lax.ppermute(local_blocks, "plane", plane_routes[offset]))
        gathered = jnp.concatenate(pieces, axis=0)
        chosen = jnp.take(gathered, remapped, axis=0)
        chosen = chosen.reshape(block_rows, -1, vec_count, 2, block_cells)
        x_re = chosen[:, :, :, 0]
        x_im = chosen[:, :, :, 1]
        expanded = jnp.stack(
            [jnp.concatenate([x_re, -x_im], axis=-1), jnp.concatenate([x_im, x_re], axis=-1)],
            axis=3,
        )
        out = jnp.einsum(
            "rkic,rkvwc->vwri", factor, expanded, preferred_element_type=jnp.float32
        )
        return out.reshape(vec_count, 2, block_rows * block_cells)

    def down_turn(turn_index, current):
        arrived = passed_along(current, "depth", 1)
        down_in = (source + coupler * arrived.astype(jnp.float32)).astype(jnp.bfloat16)
        return apply_layer(down_in).astype(jnp.bfloat16)

    first = apply_layer(source.astype(jnp.bfloat16)).astype(jnp.bfloat16)
    swept = lax.fori_loop(0, depth_count - 1, down_turn, first)

    def up_turn(turn_index, current):
        outgoing = (coupler * current.astype(jnp.float32)).astype(jnp.bfloat16)
        arrived = passed_along(outgoing, "depth", -1)
        return (swept.astype(jnp.float32) + apply_layer(arrived)).astype(jnp.bfloat16)

    precond = lax.fori_loop(0, depth_count - 1, up_turn, swept)
    product = precond.astype(jnp.float32) * toar_f32
    contrib = product[:, 0] + product[:, 1]

    cell_patch = patch_map[0]
    cell_count = cell_patch.shape[0]
    owner_count = depth_count * plane_count
    owner = cell_patch // PATCH_DEV
    hits = (owner[:, None] == jnp.arange(owner_count, dtype=owner.dtype)[None, :]).astype(jnp.int32)
    rank = jnp.take_along_axis(jnp.cumsum(hits, axis=0), owner[:, None], axis=1)[:, 0] - 1
    slot = owner * CAP + rank
    cells = jnp.arange(cell_count, dtype=jnp.int32)
    perm = jnp.full((owner_count * CAP,), cell_count, jnp.int32).at[slot].set(cells)
    local_patch = (cell_patch % PATCH_DEV).astype(jnp.float32)
    padded = jnp.concatenate(
        [jnp.concatenate([contrib.T, local_patch[:, None]], axis=1),
         jnp.zeros((1, vec_count + 1), jnp.float32)],
        axis=0,
    )
    packed = jnp.take(padded, perm, axis=0).reshape(owner_count, CAP, vec_count + 1)
    received = lax.all_to_all(packed, ("depth", "plane"), 0, 0, tiled=True)
    received = received.reshape(owner_count * CAP, vec_count + 1)
    target = received[:, vec_count].astype(jnp.int32)
    owned = jax.ops.segment_sum(received[:, :vec_count], target, num_segments=PATCH_DEV).T
    return (precond[None], owned)


def solution(mesh):
    return jax.shard_map(
        shards,
        mesh=mesh,
        in_specs=(
            P("depth", None, None, "plane"),
            P("depth", None, "plane"),
            P("depth", "plane"),
            P("depth", "plane", None, None, None),
            P("depth", "plane", None),
            P("depth", "plane"),
        ),
        out_specs=(P("depth", None, None, "plane"), P(None, ("depth", "plane"))),
        check_vma=False,
    )
```

```python
import jax
import jax.numpy as jnp
from jax import lax
from jax.sharding import PartitionSpec as P

PATCH_DEV = 128
CAP = 32


def passed_along(value, axis, steps):
    count = lax.axis_size(axis)
    first, last = (max(0, -steps), min(count, count - steps))
    return lax.ppermute(value, axis, [(source, source + steps) for source in range(first, last)])


def shards(toar, pml_coeff, coupling, inverse, pattern, patch_map):
    toar_local = toar[0]
    coeff = pml_coeff[0]
    coupler = coupling[0]
    factor = inverse[0]
    pattern_flat = pattern[0].reshape(-1)
    block_rows = factor.shape[0]
    block_cells = factor.shape[2]
    depth_count = lax.axis_size("depth")
    plane_count = lax.axis_size("plane")
    vec_count = toar_local.shape[0]
    toar_f32 = toar_local.astype(jnp.float32)
    real_part = coeff[0] * toar_f32[:, 0] - coeff[1] * toar_f32[:, 1]
    imag_part = coeff[0] * toar_f32[:, 1] + coeff[1] * toar_f32[:, 0]
    source = jnp.stack([real_part, imag_part], axis=1)

    def apply_layer(incoming):
        local_blocks = incoming.reshape(vec_count, 2, block_rows, block_cells).transpose(2, 0, 1, 3)
        local_blocks = local_blocks.reshape(block_rows, vec_count, 2 * block_cells)
        copies = jnp.broadcast_to(local_blocks[None], (plane_count,) + local_blocks.shape)
        gathered = lax.all_to_all(copies, "plane", 0, 0, tiled=True)
        gathered = gathered.reshape(plane_count * block_rows, vec_count, 2 * block_cells)
        chosen = jnp.take(gathered, pattern_flat, axis=0)
        chosen = chosen.reshape(block_rows, -1, vec_count, 2 * block_cells)
        x_re = chosen[..., :block_cells]
        x_im = chosen[..., block_cells:]
        expanded = jnp.stack(
            [jnp.concatenate([x_re, -x_im], axis=-1), jnp.concatenate([x_im, x_re], axis=-1)],
            axis=3,
        )
        out = jnp.einsum(
            "rkic,rkvwc->vwri", factor, expanded, preferred_element_type=jnp.float32
        )
        return out.reshape(vec_count, 2, block_rows * block_cells)

    def down_turn(turn_index, current):
        arrived = passed_along(current, "depth", 1)
        down_in = (source + coupler * arrived.astype(jnp.float32)).astype(jnp.bfloat16)
        return apply_layer(down_in).astype(jnp.bfloat16)

    first = apply_layer(source.astype(jnp.bfloat16)).astype(jnp.bfloat16)
    swept = lax.fori_loop(0, depth_count - 1, down_turn, first)

    def up_turn(turn_index, current):
        outgoing = (coupler * current.astype(jnp.float32)).astype(jnp.bfloat16)
        arrived = passed_along(outgoing, "depth", -1)
        return (swept.astype(jnp.float32) + apply_layer(arrived)).astype(jnp.bfloat16)

    precond = lax.fori_loop(0, depth_count - 1, up_turn, swept)
    product = precond.astype(jnp.float32) * toar_f32
    contrib = product[:, 0] + product[:, 1]

    cell_patch = patch_map[0]
    cell_count = cell_patch.shape[0]
    owner_count = depth_count * plane_count
    owner = cell_patch // PATCH_DEV
    hits = (owner[:, None] == jnp.arange(owner_count, dtype=owner.dtype)[None, :]).astype(jnp.int32)
    rank = jnp.take_along_axis(jnp.cumsum(hits, axis=0), owner[:, None], axis=1)[:, 0] - 1
    slot = owner * CAP + rank
    cells = jnp.arange(cell_count, dtype=jnp.int32)
    perm = jnp.full((owner_count * CAP,), cell_count, jnp.int32).at[slot].set(cells)
    local_patch = (cell_patch % PATCH_DEV).astype(jnp.float32)
    padded = jnp.concatenate(
        [jnp.concatenate([contrib.T, local_patch[:, None]], axis=1),
         jnp.zeros((1, vec_count + 1), jnp.float32)],
        axis=0,
    )
    packed = jnp.take(padded, perm, axis=0).reshape(owner_count, CAP, vec_count + 1)
    received = lax.all_to_all(packed, ("depth", "plane"), 0, 0, tiled=True)
    received = received.reshape(owner_count * CAP, vec_count + 1)
    target = received[:, vec_count].astype(jnp.int32)
    owned = jax.ops.segment_sum(received[:, :vec_count], target, num_segments=PATCH_DEV).T
    return (precond[None], owned)


def solution(mesh):
    return jax.shard_map(
        shards,
        mesh=mesh,
        in_specs=(
            P("depth", None, None, "plane"),
            P("depth", None, "plane"),
            P("depth", "plane"),
            P("depth", "plane", None, None, None),
            P("depth", "plane", None),
            P("depth", "plane"),
        ),
        out_specs=(P("depth", None, None, "plane"), P(None, ("depth", "plane"))),
        check_vma=False,
    )
```

```python
import jax
import jax.numpy as jnp
from jax import lax
from jax.sharding import PartitionSpec as P

PATCH_DEV = 128
CAP = 32
CHAINS = 2


def passed_along(value, axis, steps):
    count = lax.axis_size(axis)
    first, last = (max(0, -steps), min(count, count - steps))
    return lax.ppermute(value, axis, [(source, source + steps) for source in range(first, last)])


def shards(toar, pml_coeff, coupling, inverse, pattern, patch_map):
    toar_local = toar[0]
    coeff = pml_coeff[0]
    coupler = coupling[0]
    factor = inverse[0]
    pattern_flat = pattern[0].reshape(-1)
    block_rows = factor.shape[0]
    block_cells = factor.shape[2]
    depth_count = lax.axis_size("depth")
    plane_count = lax.axis_size("plane")
    vec_count = toar_local.shape[0]
    toar_f32 = toar_local.astype(jnp.float32)
    real_part = coeff[0] * toar_f32[:, 0] - coeff[1] * toar_f32[:, 1]
    imag_part = coeff[0] * toar_f32[:, 1] + coeff[1] * toar_f32[:, 0]
    source = jnp.stack([real_part, imag_part], axis=1)

    def apply_layer(incoming):
        count = incoming.shape[0]
        local_blocks = incoming.reshape(count, 2, block_rows, block_cells).transpose(2, 0, 1, 3)
        local_blocks = local_blocks.reshape(block_rows, count, 2 * block_cells)
        copies = jnp.broadcast_to(local_blocks[None], (plane_count,) + local_blocks.shape)
        gathered = lax.all_to_all(copies, "plane", 0, 0, tiled=True)
        gathered = gathered.reshape(plane_count * block_rows, count, 2 * block_cells)
        chosen = jnp.take(gathered, pattern_flat, axis=0)
        chosen = chosen.reshape(block_rows, -1, count, 2 * block_cells)
        x_re = chosen[..., :block_cells]
        x_im = chosen[..., block_cells:]
        expanded = jnp.stack(
            [jnp.concatenate([x_re, -x_im], axis=-1), jnp.concatenate([x_im, x_re], axis=-1)],
            axis=3,
        )
        out = jnp.einsum(
            "rkic,rkvwc->vwri", factor, expanded, preferred_element_type=jnp.float32
        )
        return out.reshape(count, 2, block_rows * block_cells)

    chain = vec_count // CHAINS
    spans = [slice(index * chain, (index + 1) * chain) for index in range(CHAINS)]

    def down_turn(turn_index, current):
        outs = []
        for span in spans:
            arrived = passed_along(current[span], "depth", 1)
            down_in = (source[span] + coupler * arrived.astype(jnp.float32)).astype(jnp.bfloat16)
            outs.append(apply_layer(down_in).astype(jnp.bfloat16))
        return jnp.concatenate(outs, axis=0)

    source_bf16 = source.astype(jnp.bfloat16)
    first = jnp.concatenate(
        [apply_layer(source_bf16[span]).astype(jnp.bfloat16) for span in spans], axis=0
    )
    swept = lax.fori_loop(0, depth_count - 1, down_turn, first)

    def up_turn(turn_index, current):
        outs = []
        for span in spans:
            outgoing = (coupler * current[span].astype(jnp.float32)).astype(jnp.bfloat16)
            arrived = passed_along(outgoing, "depth", -1)
            outs.append((swept[span].astype(jnp.float32) + apply_layer(arrived)).astype(jnp.bfloat16))
        return jnp.concatenate(outs, axis=0)

    precond = lax.fori_loop(0, depth_count - 1, up_turn, swept)
    product = precond.astype(jnp.float32) * toar_f32
    contrib = product[:, 0] + product[:, 1]

    cell_patch = patch_map[0]
    cell_count = cell_patch.shape[0]
    owner_count = depth_count * plane_count
    owner = cell_patch // PATCH_DEV
    hits = (owner[:, None] == jnp.arange(owner_count, dtype=owner.dtype)[None, :]).astype(jnp.int32)
    rank = jnp.take_along_axis(jnp.cumsum(hits, axis=0), owner[:, None], axis=1)[:, 0] - 1
    slot = owner * CAP + rank
    cells = jnp.arange(cell_count, dtype=jnp.int32)
    perm = jnp.full((owner_count * CAP,), cell_count, jnp.int32).at[slot].set(cells)
    local_patch = (cell_patch % PATCH_DEV).astype(jnp.float32)
    padded = jnp.concatenate(
        [jnp.concatenate([contrib.T, local_patch[:, None]], axis=1),
         jnp.zeros((1, vec_count + 1), jnp.float32)],
        axis=0,
    )
    packed = jnp.take(padded, perm, axis=0).reshape(owner_count, CAP, vec_count + 1)
    received = lax.all_to_all(packed, ("depth", "plane"), 0, 0, tiled=True)
    received = received.reshape(owner_count * CAP, vec_count + 1)
    target = received[:, vec_count].astype(jnp.int32)
    owned = jax.ops.segment_sum(received[:, :vec_count], target, num_segments=PATCH_DEV).T
    return (precond[None], owned)


def solution(mesh):
    return jax.shard_map(
        shards,
        mesh=mesh,
        in_specs=(
            P("depth", None, None, "plane"),
            P("depth", None, "plane"),
            P("depth", "plane"),
            P("depth", "plane", None, None, None),
            P("depth", "plane", None),
            P("depth", "plane"),
        ),
        out_specs=(P("depth", None, None, "plane"), P(None, ("depth", "plane"))),
        check_vma=False,
    )
```

```python
import jax
import jax.numpy as jnp
from jax import lax
from jax.sharding import PartitionSpec as P

PATCH_DEV = 128
CAP = 32


def passed_along(value, axis, steps):
    count = lax.axis_size(axis)
    first, last = (max(0, -steps), min(count, count - steps))
    return lax.ppermute(value, axis, [(source, source + steps) for source in range(first, last)])


def shards(toar, pml_coeff, coupling, inverse, pattern, patch_map):
    toar_local = toar[0]
    coeff = pml_coeff[0]
    coupler = coupling[0]
    factor = inverse[0]
    pattern_flat = pattern[0].reshape(-1)
    block_rows = factor.shape[0]
    block_cells = factor.shape[2]
    depth_count = lax.axis_size("depth")
    plane_count = lax.axis_size("plane")
    vec_count = toar_local.shape[0]
    toar_f32 = toar_local.astype(jnp.float32)
    real_part = coeff[0] * toar_f32[:, 0] - coeff[1] * toar_f32[:, 1]
    imag_part = coeff[0] * toar_f32[:, 1] + coeff[1] * toar_f32[:, 0]
    source = jnp.stack([real_part, imag_part], axis=1)

    def apply_layer(incoming):
        local_blocks = incoming.reshape(vec_count, 2, block_rows, block_cells).transpose(2, 0, 1, 3)
        local_blocks = local_blocks.reshape(block_rows, vec_count, 2 * block_cells)
        copies = jnp.broadcast_to(local_blocks[None], (plane_count,) + local_blocks.shape)
        gathered = lax.all_to_all(copies, "plane", 0, 0, tiled=True)
        gathered = gathered.reshape(plane_count * block_rows, vec_count, 2 * block_cells)
        chosen = jnp.take(gathered, pattern_flat, axis=0, mode="clip")
        chosen = chosen.reshape(block_rows, -1, vec_count, 2 * block_cells)
        x_re = chosen[..., :block_cells]
        x_im = chosen[..., block_cells:]
        expanded = jnp.stack(
            [jnp.concatenate([x_re, -x_im], axis=-1), jnp.concatenate([x_im, x_re], axis=-1)],
            axis=3,
        )
        out = jnp.einsum(
            "rkic,rkvwc->vwri", factor, expanded, preferred_element_type=jnp.float32
        )
        return out.reshape(vec_count, 2, block_rows * block_cells)

    def down_turn(turn_index, current):
        arrived = passed_along(current, "depth", 1)
        down_in = (source + coupler * arrived.astype(jnp.float32)).astype(jnp.bfloat16)
        return apply_layer(down_in).astype(jnp.bfloat16)

    first = apply_layer(source.astype(jnp.bfloat16)).astype(jnp.bfloat16)
    swept = lax.fori_loop(0, depth_count - 1, down_turn, first)

    def up_turn(turn_index, current):
        outgoing = (coupler * current.astype(jnp.float32)).astype(jnp.bfloat16)
        arrived = passed_along(outgoing, "depth", -1)
        return (swept.astype(jnp.float32) + apply_layer(arrived)).astype(jnp.bfloat16)

    precond = lax.fori_loop(0, depth_count - 1, up_turn, swept)
    product = precond.astype(jnp.float32) * toar_f32
    contrib = product[:, 0] + product[:, 1]

    cell_patch = patch_map[0]
    cell_count = cell_patch.shape[0]
    owner_count = depth_count * plane_count
    owner = cell_patch // PATCH_DEV
    hits = (owner[:, None] == jnp.arange(owner_count, dtype=owner.dtype)[None, :]).astype(jnp.bfloat16)
    cells = jnp.arange(cell_count, dtype=jnp.int32)
    lower = (cells[:, None] >= cells[None, :]).astype(jnp.bfloat16)
    running = jnp.dot(lower, hits, preferred_element_type=jnp.float32)
    rank = jnp.sum(running * hits.astype(jnp.float32), axis=1).astype(jnp.int32) - 1
    slot = owner * CAP + rank
    perm = jnp.full((owner_count * CAP,), cell_count, jnp.int32).at[slot].set(cells)
    local_patch = (cell_patch % PATCH_DEV).astype(jnp.float32)
    padded = jnp.concatenate(
        [jnp.concatenate([contrib.T, local_patch[:, None]], axis=1),
         jnp.zeros((1, vec_count + 1), jnp.float32)],
        axis=0,
    )
    packed = jnp.take(padded, perm, axis=0, mode="clip").reshape(owner_count, CAP, vec_count + 1)
    received = lax.all_to_all(packed, ("depth", "plane"), 0, 0, tiled=True)
    received = received.reshape(owner_count * CAP, vec_count + 1)
    target = received[:, vec_count].astype(jnp.int32)
    choose = (target[:, None] == jnp.arange(PATCH_DEV, dtype=jnp.int32)[None, :]).astype(jnp.float32)
    owned = jnp.einsum(
        "sv,sp->vp", received[:, :vec_count], choose, precision=lax.Precision.HIGHEST,
        preferred_element_type=jnp.float32,
    )
    return (precond[None], owned)


def solution(mesh):
    return jax.shard_map(
        shards,
        mesh=mesh,
        in_specs=(
            P("depth", None, None, "plane"),
            P("depth", None, "plane"),
            P("depth", "plane"),
            P("depth", "plane", None, None, None),
            P("depth", "plane", None),
            P("depth", "plane"),
        ),
        out_specs=(P("depth", None, None, "plane"), P(None, ("depth", "plane"))),
        check_vma=False,
    )
```

```python
import jax
import jax.numpy as jnp
from jax import lax
from jax.sharding import PartitionSpec as P

PATCH_DEV = 128
CAP = 32


def passed_along(value, axis, steps):
    count = lax.axis_size(axis)
    first, last = (max(0, -steps), min(count, count - steps))
    return lax.ppermute(value, axis, [(source, source + steps) for source in range(first, last)])


def shards(toar, pml_coeff, coupling, inverse, pattern, patch_map):
    toar_local = toar[0]
    coeff = pml_coeff[0]
    coupler = coupling[0]
    factor = inverse[0]
    pattern_flat = pattern[0].reshape(-1)
    block_rows = factor.shape[0]
    block_cells = factor.shape[2]
    depth_count = lax.axis_size("depth")
    plane_count = lax.axis_size("plane")
    vec_count = toar_local.shape[0]
    toar_f32 = toar_local.astype(jnp.float32)
    real_part = coeff[0] * toar_f32[:, 0] - coeff[1] * toar_f32[:, 1]
    imag_part = coeff[0] * toar_f32[:, 1] + coeff[1] * toar_f32[:, 0]
    source = jnp.stack([real_part, imag_part], axis=1)

    def apply_layer(incoming):
        local_blocks = incoming.reshape(vec_count, 2, block_rows, block_cells).transpose(2, 0, 1, 3)
        local_blocks = local_blocks.reshape(block_rows, vec_count, 2 * block_cells)
        copies = jnp.broadcast_to(local_blocks[None], (plane_count,) + local_blocks.shape)
        gathered = lax.all_to_all(copies, "plane", 0, 0, tiled=True)
        gathered = gathered.reshape(plane_count * block_rows, vec_count, 2 * block_cells)
        chosen = jnp.take(gathered, pattern_flat, axis=0, mode="clip")
        chosen = chosen.reshape(block_rows, -1, vec_count, 2 * block_cells)
        x_re = chosen[..., :block_cells]
        x_im = chosen[..., block_cells:]
        expanded = jnp.stack(
            [jnp.concatenate([x_re, -x_im], axis=-1), jnp.concatenate([x_im, x_re], axis=-1)],
            axis=3,
        )
        out = jnp.einsum(
            "rkic,rkvwc->vwri", factor, expanded, preferred_element_type=jnp.float32
        )
        return out.reshape(vec_count, 2, block_rows * block_cells)

    def down_turn(turn_index, current):
        arrived = passed_along(current, "depth", 1)
        down_in = (source + coupler * arrived.astype(jnp.float32)).astype(jnp.bfloat16)
        return apply_layer(down_in).astype(jnp.bfloat16)

    first = apply_layer(source.astype(jnp.bfloat16)).astype(jnp.bfloat16)
    swept = lax.fori_loop(0, depth_count - 1, down_turn, first)

    def up_turn(turn_index, current):
        outgoing = (coupler * current.astype(jnp.float32)).astype(jnp.bfloat16)
        arrived = passed_along(outgoing, "depth", -1)
        return (swept.astype(jnp.float32) + apply_layer(arrived)).astype(jnp.bfloat16)

    precond = lax.fori_loop(0, depth_count - 1, up_turn, swept)
    product = precond.astype(jnp.float32) * toar_f32
    contrib = product[:, 0] + product[:, 1]

    cell_patch = patch_map[0]
    cell_count = cell_patch.shape[0]
    owner_count = depth_count * plane_count
    owner = cell_patch // PATCH_DEV
    hits = (owner[:, None] == jnp.arange(owner_count, dtype=owner.dtype)[None, :]).astype(jnp.bfloat16)
    cells = jnp.arange(cell_count, dtype=jnp.int32)
    lower = (cells[:, None] >= cells[None, :]).astype(jnp.bfloat16)
    running = jnp.dot(lower, hits, preferred_element_type=jnp.float32)
    rank = jnp.sum(running * hits.astype(jnp.float32), axis=1).astype(jnp.int32) - 1
    slot = owner * CAP + rank
    placed = (slot[:, None] == jnp.arange(owner_count * CAP, dtype=jnp.int32)[None, :]).astype(jnp.bfloat16)
    local_patch = (cell_patch % PATCH_DEV).astype(jnp.float32)
    rows = jnp.concatenate([contrib.T, local_patch[:, None]], axis=1)
    high = rows.astype(jnp.bfloat16)
    rest = rows - high.astype(jnp.float32)
    middle = rest.astype(jnp.bfloat16)
    low = (rest - middle.astype(jnp.float32)).astype(jnp.bfloat16)
    parts = jnp.concatenate([high, middle, low], axis=1)
    moved = jnp.einsum("cs,cq->sq", placed, parts, preferred_element_type=jnp.float32)
    width = vec_count + 1
    packed = (moved[:, :width] + moved[:, width:2 * width]) + moved[:, 2 * width:]
    packed = packed.reshape(owner_count, CAP, width)
    received = lax.all_to_all(packed, ("depth", "plane"), 0, 0, tiled=True)
    received = received.reshape(owner_count * CAP, vec_count + 1)
    target = received[:, vec_count].astype(jnp.int32)
    choose = (target[:, None] == jnp.arange(PATCH_DEV, dtype=jnp.int32)[None, :]).astype(jnp.float32)
    owned = jnp.einsum(
        "sv,sp->vp", received[:, :vec_count], choose, precision=lax.Precision.HIGHEST,
        preferred_element_type=jnp.float32,
    )
    return (precond[None], owned)


def solution(mesh):
    return jax.shard_map(
        shards,
        mesh=mesh,
        in_specs=(
            P("depth", None, None, "plane"),
            P("depth", None, "plane"),
            P("depth", "plane"),
            P("depth", "plane", None, None, None),
            P("depth", "plane", None),
            P("depth", "plane"),
        ),
        out_specs=(P("depth", None, None, "plane"), P(None, ("depth", "plane"))),
        check_vma=False,
    )
```

```python
import jax
import jax.numpy as jnp
from jax import lax
from jax.sharding import PartitionSpec as P

PATCH_DEV = 128
CAP = 32


def passed_along(value, axis, steps):
    count = lax.axis_size(axis)
    first, last = (max(0, -steps), min(count, count - steps))
    return lax.ppermute(value, axis, [(source, source + steps) for source in range(first, last)])


def shards(toar, pml_coeff, coupling, inverse, pattern, patch_map):
    toar_local = toar[0]
    coeff = pml_coeff[0]
    coupler = coupling[0]
    factor = inverse[0]
    pattern_flat = pattern[0].reshape(-1)
    block_rows = factor.shape[0]
    block_cells = factor.shape[2]
    depth_count = lax.axis_size("depth")
    plane_count = lax.axis_size("plane")
    vec_count = toar_local.shape[0]
    toar_f32 = toar_local.astype(jnp.float32)
    real_part = coeff[0] * toar_f32[:, 0] - coeff[1] * toar_f32[:, 1]
    imag_part = coeff[0] * toar_f32[:, 1] + coeff[1] * toar_f32[:, 0]
    source = jnp.stack([real_part, imag_part], axis=1)

    def apply_layer(incoming):
        local_blocks = incoming.reshape(vec_count, 2, block_rows, block_cells).transpose(2, 0, 1, 3)
        local_blocks = local_blocks.reshape(block_rows, vec_count, 2 * block_cells)
        copies = jnp.broadcast_to(local_blocks[None], (plane_count,) + local_blocks.shape)
        gathered = lax.all_to_all(copies, "plane", 0, 0, tiled=True)
        gathered = gathered.reshape(plane_count * block_rows, vec_count, 2 * block_cells)
        chosen = jnp.take(gathered, pattern_flat, axis=0, mode="clip")
        chosen = chosen.reshape(block_rows, -1, vec_count, 2 * block_cells)
        x_re = chosen[..., :block_cells]
        x_im = chosen[..., block_cells:]
        expanded = jnp.stack(
            [jnp.concatenate([x_re, -x_im], axis=-1), jnp.concatenate([x_im, x_re], axis=-1)],
            axis=3,
        )
        out = jnp.einsum(
            "rkic,rkvwc->vwri", factor, expanded, preferred_element_type=jnp.float32
        )
        return out.reshape(vec_count, 2, block_rows * block_cells)

    def down_turn(turn_index, current):
        arrived = passed_along(current, "depth", 1)
        down_in = (source + coupler * arrived.astype(jnp.float32)).astype(jnp.bfloat16)
        return apply_layer(down_in).astype(jnp.bfloat16)

    first = apply_layer(source.astype(jnp.bfloat16)).astype(jnp.bfloat16)
    swept = lax.fori_loop(0, depth_count - 1, down_turn, first)

    def up_turn(turn_index, current):
        outgoing = (coupler * current.astype(jnp.float32)).astype(jnp.bfloat16)
        arrived = passed_along(outgoing, "depth", -1)
        return (swept.astype(jnp.float32) + apply_layer(arrived)).astype(jnp.bfloat16)

    precond = lax.fori_loop(0, depth_count - 1, up_turn, swept)
    product = precond.astype(jnp.float32) * toar_f32
    contrib = product[:, 0] + product[:, 1]

    cell_patch = patch_map[0]
    cell_count = cell_patch.shape[0]
    owner_count = depth_count * plane_count
    owner = cell_patch // PATCH_DEV
    hits = (owner[:, None] == jnp.arange(owner_count, dtype=owner.dtype)[None, :]).astype(jnp.bfloat16)
    cells = jnp.arange(cell_count, dtype=jnp.int32)
    lower = (cells[:, None] >= cells[None, :]).astype(jnp.bfloat16)
    running = jnp.dot(lower, hits, preferred_element_type=jnp.float32)
    rank = jnp.sum(running * hits.astype(jnp.float32), axis=1).astype(jnp.int32) - 1
    slot = owner * CAP + rank
    placed = (slot[:, None] == jnp.arange(owner_count * CAP, dtype=jnp.int32)[None, :]).astype(jnp.bfloat16)
    local_patch = (cell_patch % PATCH_DEV).astype(jnp.float32)
    rows = jnp.concatenate([contrib.T, local_patch[:, None]], axis=1)
    high = lax.reduce_precision(rows, exponent_bits=8, mantissa_bits=7)
    rest = rows - high
    middle = lax.reduce_precision(rest, exponent_bits=8, mantissa_bits=7)
    low = rest - middle
    parts = jnp.concatenate([high, middle, low], axis=1).astype(jnp.bfloat16)
    moved = jnp.einsum("cs,cq->sq", placed, parts, preferred_element_type=jnp.float32)
    width = vec_count + 1
    packed = (moved[:, :width] + moved[:, width:2 * width]) + moved[:, 2 * width:]
    packed = packed.reshape(owner_count, CAP, width)
    received = lax.all_to_all(packed, ("depth", "plane"), 0, 0, tiled=True)
    received = received.reshape(owner_count * CAP, vec_count + 1)
    target = received[:, vec_count].astype(jnp.int32)
    choose = (target[:, None] == jnp.arange(PATCH_DEV, dtype=jnp.int32)[None, :]).astype(jnp.float32)
    owned = jnp.einsum(
        "sv,sp->vp", received[:, :vec_count], choose, precision=lax.Precision.HIGHEST,
        preferred_element_type=jnp.float32,
    )
    return (precond[None], owned)


def solution(mesh):
    return jax.shard_map(
        shards,
        mesh=mesh,
        in_specs=(
            P("depth", None, None, "plane"),
            P("depth", None, "plane"),
            P("depth", "plane"),
            P("depth", "plane", None, None, None),
            P("depth", "plane", None),
            P("depth", "plane"),
        ),
        out_specs=(P("depth", None, None, "plane"), P(None, ("depth", "plane"))),
        check_vma=False,
    )
```

```python
import jax
import jax.numpy as jnp
from jax import lax
from jax.sharding import PartitionSpec as P

PATCH_DEV = 128
CAP = 32


def passed_along(value, axis, steps):
    count = lax.axis_size(axis)
    first, last = (max(0, -steps), min(count, count - steps))
    return lax.ppermute(value, axis, [(source, source + steps) for source in range(first, last)])


def shards(toar, pml_coeff, coupling, inverse, pattern, patch_map):
    toar_local = toar[0]
    coeff = pml_coeff[0]
    coupler = coupling[0]
    factor = inverse[0]
    pattern_flat = pattern[0].reshape(-1)
    block_rows = factor.shape[0]
    block_cells = factor.shape[2]
    depth_count = lax.axis_size("depth")
    plane_count = lax.axis_size("plane")
    vec_count = toar_local.shape[0]
    toar_f32 = toar_local.astype(jnp.float32)
    real_part = coeff[0] * toar_f32[:, 0] - coeff[1] * toar_f32[:, 1]
    imag_part = coeff[0] * toar_f32[:, 1] + coeff[1] * toar_f32[:, 0]
    source = jnp.stack([real_part, imag_part], axis=1)

    lanes = jnp.arange(2 * block_cells)
    flip = jnp.where(lanes < block_cells, 1.0, -1.0).astype(factor.dtype)
    paired = jnp.stack([factor * flip, jnp.roll(factor, block_cells, axis=-1)], axis=2)

    def apply_layer(incoming):
        local_blocks = incoming.reshape(vec_count, 2, block_rows, block_cells).transpose(2, 0, 1, 3)
        local_blocks = local_blocks.reshape(block_rows, vec_count, 2 * block_cells)
        copies = jnp.broadcast_to(local_blocks[None], (plane_count,) + local_blocks.shape)
        gathered = lax.all_to_all(copies, "plane", 0, 0, tiled=True)
        gathered = gathered.reshape(plane_count * block_rows, vec_count, 2 * block_cells)
        chosen = jnp.take(gathered, pattern_flat, axis=0, mode="clip")
        chosen = chosen.reshape(block_rows, -1, vec_count, 2 * block_cells)
        out = jnp.einsum(
            "rkwic,rkvc->vwri", paired, chosen, preferred_element_type=jnp.float32
        )
        return out.reshape(vec_count, 2, block_rows * block_cells)

    def down_turn(turn_index, current):
        arrived = passed_along(current, "depth", 1)
        down_in = (source + coupler * arrived.astype(jnp.float32)).astype(jnp.bfloat16)
        return apply_layer(down_in).astype(jnp.bfloat16)

    first = apply_layer(source.astype(jnp.bfloat16)).astype(jnp.bfloat16)
    swept = lax.fori_loop(0, depth_count - 1, down_turn, first)

    def up_turn(turn_index, current):
        outgoing = (coupler * current.astype(jnp.float32)).astype(jnp.bfloat16)
        arrived = passed_along(outgoing, "depth", -1)
        return (swept.astype(jnp.float32) + apply_layer(arrived)).astype(jnp.bfloat16)

    precond = lax.fori_loop(0, depth_count - 1, up_turn, swept)
    product = precond.astype(jnp.float32) * toar_f32
    contrib = product[:, 0] + product[:, 1]

    cell_patch = patch_map[0]
    cell_count = cell_patch.shape[0]
    owner_count = depth_count * plane_count
    owner = cell_patch // PATCH_DEV
    hits = (owner[:, None] == jnp.arange(owner_count, dtype=owner.dtype)[None, :]).astype(jnp.bfloat16)
    cells = jnp.arange(cell_count, dtype=jnp.int32)
    lower = (cells[:, None] >= cells[None, :]).astype(jnp.bfloat16)
    running = jnp.dot(lower, hits, preferred_element_type=jnp.float32)
    rank = jnp.sum(running * hits.astype(jnp.float32), axis=1).astype(jnp.int32) - 1
    slot = owner * CAP + rank
    placed = (slot[:, None] == jnp.arange(owner_count * CAP, dtype=jnp.int32)[None, :]).astype(jnp.bfloat16)
    local_patch = (cell_patch % PATCH_DEV).astype(jnp.float32)
    rows = jnp.concatenate([contrib.T, local_patch[:, None]], axis=1)
    high = lax.reduce_precision(rows, exponent_bits=8, mantissa_bits=7)
    rest = rows - high
    middle = lax.reduce_precision(rest, exponent_bits=8, mantissa_bits=7)
    low = rest - middle
    parts = jnp.concatenate([high, middle, low], axis=1).astype(jnp.bfloat16)
    moved = jnp.einsum("cs,cq->sq", placed, parts, preferred_element_type=jnp.float32)
    width = vec_count + 1
    packed = (moved[:, :width] + moved[:, width:2 * width]) + moved[:, 2 * width:]
    packed = packed.reshape(owner_count, CAP, width)
    received = lax.all_to_all(packed, ("depth", "plane"), 0, 0, tiled=True)
    received = received.reshape(owner_count * CAP, vec_count + 1)
    target = received[:, vec_count].astype(jnp.int32)
    choose = (target[:, None] == jnp.arange(PATCH_DEV, dtype=jnp.int32)[None, :]).astype(jnp.float32)
    owned = jnp.einsum(
        "sv,sp->vp", received[:, :vec_count], choose, precision=lax.Precision.HIGHEST,
        preferred_element_type=jnp.float32,
    )
    return (precond[None], owned)


def solution(mesh):
    return jax.shard_map(
        shards,
        mesh=mesh,
        in_specs=(
            P("depth", None, None, "plane"),
            P("depth", None, "plane"),
            P("depth", "plane"),
            P("depth", "plane", None, None, None),
            P("depth", "plane", None),
            P("depth", "plane"),
        ),
        out_specs=(P("depth", None, None, "plane"), P(None, ("depth", "plane"))),
        check_vma=False,
    )
```

```python
import jax
import jax.numpy as jnp
from jax import lax
from jax.sharding import PartitionSpec as P

PATCH_DEV = 128
CAP = 32


def passed_along(value, axis, steps):
    count = lax.axis_size(axis)
    first, last = (max(0, -steps), min(count, count - steps))
    return lax.ppermute(value, axis, [(source, source + steps) for source in range(first, last)])


def shards(toar, pml_coeff, coupling, inverse, pattern, patch_map):
    toar_local = toar[0]
    coeff = pml_coeff[0]
    coupler = coupling[0]
    factor = inverse[0]
    pattern_flat = pattern[0].reshape(-1)
    block_rows = factor.shape[0]
    block_cells = factor.shape[2]
    depth_count = lax.axis_size("depth")
    plane_count = lax.axis_size("plane")
    vec_count = toar_local.shape[0]
    toar_f32 = toar_local.astype(jnp.float32)
    real_part = coeff[0] * toar_f32[:, 0] - coeff[1] * toar_f32[:, 1]
    imag_part = coeff[0] * toar_f32[:, 1] + coeff[1] * toar_f32[:, 0]
    source = jnp.stack([real_part, imag_part], axis=1)

    def apply_layer(incoming):
        local_blocks = incoming.reshape(vec_count, 2, block_rows, block_cells).transpose(2, 0, 1, 3)
        local_blocks = local_blocks.reshape(block_rows, vec_count, 2 * block_cells)
        copies = jnp.broadcast_to(local_blocks[None], (plane_count,) + local_blocks.shape)
        gathered = lax.all_to_all(copies, "plane", 0, 0, tiled=True)
        gathered = gathered.reshape(plane_count * block_rows, vec_count, 2 * block_cells)
        chosen = jnp.take(gathered, pattern_flat, axis=0, mode="clip")
        chosen = chosen.reshape(block_rows, -1, vec_count, 2 * block_cells)
        x_re = chosen[..., :block_cells]
        x_im = chosen[..., block_cells:]
        expanded = jnp.stack(
            [jnp.concatenate([x_re, -x_im], axis=-1), jnp.concatenate([x_im, x_re], axis=-1)],
            axis=3,
        )
        out = jnp.einsum(
            "rkic,rkvwc->vwri", factor, expanded, preferred_element_type=jnp.float32
        )
        return out.reshape(vec_count, 2, block_rows * block_cells)

    def down_turn(turn_index, current):
        arrived = passed_along(current, "depth", 1)
        down_in = (source + coupler * arrived.astype(jnp.float32)).astype(jnp.bfloat16)
        return apply_layer(down_in).astype(jnp.bfloat16)

    swept = apply_layer(source.astype(jnp.bfloat16)).astype(jnp.bfloat16)
    for turn_index in range(depth_count - 1):
        swept = down_turn(turn_index, swept)

    def up_turn(turn_index, current):
        outgoing = (coupler * current.astype(jnp.float32)).astype(jnp.bfloat16)
        arrived = passed_along(outgoing, "depth", -1)
        return (swept.astype(jnp.float32) + apply_layer(arrived)).astype(jnp.bfloat16)

    precond = swept
    for turn_index in range(depth_count - 1):
        precond = up_turn(turn_index, precond)
    product = precond.astype(jnp.float32) * toar_f32
    contrib = product[:, 0] + product[:, 1]

    cell_patch = patch_map[0]
    cell_count = cell_patch.shape[0]
    owner_count = depth_count * plane_count
    owner = cell_patch // PATCH_DEV
    hits = (owner[:, None] == jnp.arange(owner_count, dtype=owner.dtype)[None, :]).astype(jnp.bfloat16)
    cells = jnp.arange(cell_count, dtype=jnp.int32)
    lower = (cells[:, None] >= cells[None, :]).astype(jnp.bfloat16)
    running = jnp.dot(lower, hits, preferred_element_type=jnp.float32)
    rank = jnp.sum(running * hits.astype(jnp.float32), axis=1).astype(jnp.int32) - 1
    slot = owner * CAP + rank
    placed = (slot[:, None] == jnp.arange(owner_count * CAP, dtype=jnp.int32)[None, :]).astype(jnp.bfloat16)
    local_patch = (cell_patch % PATCH_DEV).astype(jnp.float32)
    rows = jnp.concatenate([contrib.T, local_patch[:, None]], axis=1)
    high = lax.reduce_precision(rows, exponent_bits=8, mantissa_bits=7)
    rest = rows - high
    middle = lax.reduce_precision(rest, exponent_bits=8, mantissa_bits=7)
    low = rest - middle
    parts = jnp.concatenate([high, middle, low], axis=1).astype(jnp.bfloat16)
    moved = jnp.einsum("cs,cq->sq", placed, parts, preferred_element_type=jnp.float32)
    width = vec_count + 1
    packed = (moved[:, :width] + moved[:, width:2 * width]) + moved[:, 2 * width:]
    packed = packed.reshape(owner_count, CAP, width)
    received = lax.all_to_all(packed, ("depth", "plane"), 0, 0, tiled=True)
    received = received.reshape(owner_count * CAP, vec_count + 1)
    target = received[:, vec_count].astype(jnp.int32)
    choose = (target[:, None] == jnp.arange(PATCH_DEV, dtype=jnp.int32)[None, :]).astype(jnp.float32)
    owned = jnp.einsum(
        "sv,sp->vp", received[:, :vec_count], choose, precision=lax.Precision.HIGHEST,
        preferred_element_type=jnp.float32,
    )
    return (precond[None], owned)


def solution(mesh):
    return jax.shard_map(
        shards,
        mesh=mesh,
        in_specs=(
            P("depth", None, None, "plane"),
            P("depth", None, "plane"),
            P("depth", "plane"),
            P("depth", "plane", None, None, None),
            P("depth", "plane", None),
            P("depth", "plane"),
        ),
        out_specs=(P("depth", None, None, "plane"), P(None, ("depth", "plane"))),
        check_vma=False,
    )
```

```python
import jax
import jax.numpy as jnp
from jax import lax
from jax.sharding import PartitionSpec as P

PATCH_DEV = 128
CAP = 32


def passed_along(value, axis, steps):
    count = lax.axis_size(axis)
    first, last = (max(0, -steps), min(count, count - steps))
    return lax.ppermute(value, axis, [(source, source + steps) for source in range(first, last)])


def shards(toar, pml_coeff, coupling, inverse, pattern, patch_map):
    toar_local = toar[0]
    coeff = pml_coeff[0]
    coupler = coupling[0]
    factor = inverse[0]
    pattern_flat = pattern[0].reshape(-1)
    block_rows = factor.shape[0]
    block_cells = factor.shape[2]
    depth_count = lax.axis_size("depth")
    plane_count = lax.axis_size("plane")
    vec_count = toar_local.shape[0]
    toar_f32 = toar_local.astype(jnp.float32)
    real_part = coeff[0] * toar_f32[:, 0] - coeff[1] * toar_f32[:, 1]
    imag_part = coeff[0] * toar_f32[:, 1] + coeff[1] * toar_f32[:, 0]
    source = jnp.stack([real_part, imag_part], axis=1)

    def apply_layer(incoming):
        local_blocks = incoming.reshape(vec_count, 2, block_rows, block_cells).transpose(2, 0, 1, 3)
        local_blocks = local_blocks.reshape(block_rows, vec_count, 2 * block_cells)
        copies = jnp.broadcast_to(local_blocks[None], (plane_count,) + local_blocks.shape)
        gathered = lax.all_to_all(copies, "plane", 0, 0, tiled=True)
        gathered = gathered.reshape(plane_count * block_rows, vec_count, 2 * block_cells)
        chosen = jnp.take(gathered, pattern_flat, axis=0, mode="clip")
        chosen = chosen.reshape(block_rows, -1, vec_count, 2 * block_cells)
        x_re = chosen[..., :block_cells]
        x_im = chosen[..., block_cells:]
        expanded = jnp.stack(
            [jnp.concatenate([x_re, -x_im], axis=-1), jnp.concatenate([x_im, x_re], axis=-1)],
            axis=3,
        )
        out = jnp.einsum(
            "rkic,rkvwc->vwri", factor, expanded, preferred_element_type=jnp.float32
        )
        return out.reshape(vec_count, 2, block_rows * block_cells)

    def down_turn(turn_index, current):
        arrived = passed_along(current, "depth", 1)
        down_in = (source + coupler * arrived.astype(jnp.float32)).astype(jnp.bfloat16)
        return apply_layer(down_in).astype(jnp.bfloat16)

    swept = apply_layer(source.astype(jnp.bfloat16)).astype(jnp.bfloat16)
    for turn_index in range(depth_count - 1):
        swept = down_turn(turn_index, swept)

    def up_turn(turn_index, current):
        outgoing = (coupler * current.astype(jnp.float32)).astype(jnp.bfloat16)
        arrived = passed_along(outgoing, "depth", -1)
        return (swept.astype(jnp.float32) + apply_layer(arrived)).astype(jnp.bfloat16)

    precond = swept
    for turn_index in range(depth_count - 1):
        precond = up_turn(turn_index, precond)
    product = precond.astype(jnp.float32) * toar_f32
    contrib = product[:, 0] + product[:, 1]

    cell_patch = patch_map[0]
    cell_count = cell_patch.shape[0]
    owner_count = depth_count * plane_count
    owner = cell_patch // PATCH_DEV
    hits = (owner[:, None] == jnp.arange(owner_count, dtype=owner.dtype)[None, :]).astype(jnp.bfloat16)
    cells = jnp.arange(cell_count, dtype=jnp.int32)
    lower = (cells[:, None] >= cells[None, :]).astype(jnp.bfloat16)
    running = jnp.dot(lower, hits, preferred_element_type=jnp.float32)
    rank = jnp.sum(running * hits.astype(jnp.float32), axis=1).astype(jnp.int32) - 1
    by_owner = hits
    by_rank = (rank[:, None] == jnp.arange(CAP, dtype=jnp.int32)[None, :]).astype(jnp.bfloat16)
    local_patch = (cell_patch % PATCH_DEV).astype(jnp.float32)
    rows = jnp.concatenate([contrib.T, local_patch[:, None]], axis=1)
    high = lax.reduce_precision(rows, exponent_bits=8, mantissa_bits=7)
    rest = rows - high
    middle = lax.reduce_precision(rest, exponent_bits=8, mantissa_bits=7)
    low = rest - middle
    parts = jnp.concatenate([high, middle, low], axis=1).astype(jnp.bfloat16)
    spread = (by_rank[:, :, None] * parts[:, None, :]).reshape(cell_count, -1)
    moved = jnp.einsum("co,cq->oq", by_owner, spread, preferred_element_type=jnp.float32)
    moved = moved.reshape(owner_count * CAP, -1)
    width = vec_count + 1
    packed = (moved[:, :width] + moved[:, width:2 * width]) + moved[:, 2 * width:]
    packed = packed.reshape(owner_count, CAP, width)
    received = lax.all_to_all(packed, ("depth", "plane"), 0, 0, tiled=True)
    received = received.reshape(owner_count * CAP, vec_count + 1)
    target = received[:, vec_count].astype(jnp.int32)
    choose = (target[:, None] == jnp.arange(PATCH_DEV, dtype=jnp.int32)[None, :]).astype(jnp.float32)
    owned = jnp.einsum(
        "sv,sp->vp", received[:, :vec_count], choose, precision=lax.Precision.HIGHEST,
        preferred_element_type=jnp.float32,
    )
    return (precond[None], owned)


def solution(mesh):
    return jax.shard_map(
        shards,
        mesh=mesh,
        in_specs=(
            P("depth", None, None, "plane"),
            P("depth", None, "plane"),
            P("depth", "plane"),
            P("depth", "plane", None, None, None),
            P("depth", "plane", None),
            P("depth", "plane"),
        ),
        out_specs=(P("depth", None, None, "plane"), P(None, ("depth", "plane"))),
        check_vma=False,
    )
```

```python
import jax
import jax.numpy as jnp
from jax import lax
from jax.sharding import PartitionSpec as P

PATCH_DEV = 128
CAP = 32


def passed_along(value, axis, steps):
    count = lax.axis_size(axis)
    moved = lax.ppermute(value, axis, [(source, (source + steps) % count) for source in range(count)])
    target = lax.axis_index(axis) - steps
    keep = (target >= 0) & (target < count)
    return jnp.where(keep, moved, jnp.zeros_like(moved))


def shards(toar, pml_coeff, coupling, inverse, pattern, patch_map):
    toar_local = toar[0]
    coeff = pml_coeff[0]
    coupler = coupling[0]
    factor = inverse[0]
    pattern_flat = pattern[0].reshape(-1)
    block_rows = factor.shape[0]
    block_cells = factor.shape[2]
    depth_count = lax.axis_size("depth")
    plane_count = lax.axis_size("plane")
    vec_count = toar_local.shape[0]
    toar_f32 = toar_local.astype(jnp.float32)
    real_part = coeff[0] * toar_f32[:, 0] - coeff[1] * toar_f32[:, 1]
    imag_part = coeff[0] * toar_f32[:, 1] + coeff[1] * toar_f32[:, 0]
    source = jnp.stack([real_part, imag_part], axis=1)

    def apply_layer(incoming):
        local_blocks = incoming.reshape(vec_count, 2, block_rows, block_cells).transpose(2, 0, 1, 3)
        local_blocks = local_blocks.reshape(block_rows, vec_count, 2 * block_cells)
        copies = jnp.broadcast_to(local_blocks[None], (plane_count,) + local_blocks.shape)
        gathered = lax.all_to_all(copies, "plane", 0, 0, tiled=True)
        gathered = gathered.reshape(plane_count * block_rows, vec_count, 2 * block_cells)
        chosen = jnp.take(gathered, pattern_flat, axis=0, mode="clip")
        chosen = chosen.reshape(block_rows, -1, vec_count, 2 * block_cells)
        x_re = chosen[..., :block_cells]
        x_im = chosen[..., block_cells:]
        expanded = jnp.stack(
            [jnp.concatenate([x_re, -x_im], axis=-1), jnp.concatenate([x_im, x_re], axis=-1)],
            axis=3,
        )
        out = jnp.einsum(
            "rkic,rkvwc->vwri", factor, expanded, preferred_element_type=jnp.float32
        )
        return out.reshape(vec_count, 2, block_rows * block_cells)

    def down_turn(turn_index, current):
        arrived = passed_along(current, "depth", 1)
        down_in = (source + coupler * arrived.astype(jnp.float32)).astype(jnp.bfloat16)
        return apply_layer(down_in).astype(jnp.bfloat16)

    swept = apply_layer(source.astype(jnp.bfloat16)).astype(jnp.bfloat16)
    for turn_index in range(depth_count - 1):
        swept = down_turn(turn_index, swept)

    def up_turn(turn_index, current):
        outgoing = (coupler * current.astype(jnp.float32)).astype(jnp.bfloat16)
        arrived = passed_along(outgoing, "depth", -1)
        return (swept.astype(jnp.float32) + apply_layer(arrived)).astype(jnp.bfloat16)

    precond = swept
    for turn_index in range(depth_count - 1):
        precond = up_turn(turn_index, precond)
    product = precond.astype(jnp.float32) * toar_f32
    contrib = product[:, 0] + product[:, 1]

    cell_patch = patch_map[0]
    cell_count = cell_patch.shape[0]
    owner_count = depth_count * plane_count
    owner = cell_patch // PATCH_DEV
    hits = (owner[:, None] == jnp.arange(owner_count, dtype=owner.dtype)[None, :]).astype(jnp.bfloat16)
    cells = jnp.arange(cell_count, dtype=jnp.int32)
    lower = (cells[:, None] >= cells[None, :]).astype(jnp.bfloat16)
    running = jnp.dot(lower, hits, preferred_element_type=jnp.float32)
    rank = jnp.sum(running * hits.astype(jnp.float32), axis=1).astype(jnp.int32) - 1
    slot = owner * CAP + rank
    placed = (slot[:, None] == jnp.arange(owner_count * CAP, dtype=jnp.int32)[None, :]).astype(jnp.bfloat16)
    local_patch = (cell_patch % PATCH_DEV).astype(jnp.float32)
    rows = jnp.concatenate([contrib.T, local_patch[:, None]], axis=1)
    high = lax.reduce_precision(rows, exponent_bits=8, mantissa_bits=7)
    rest = rows - high
    middle = lax.reduce_precision(rest, exponent_bits=8, mantissa_bits=7)
    low = rest - middle
    parts = jnp.concatenate([high, middle, low], axis=1).astype(jnp.bfloat16)
    moved = jnp.einsum("cs,cq->sq", placed, parts, preferred_element_type=jnp.float32)
    width = vec_count + 1
    packed = (moved[:, :width] + moved[:, width:2 * width]) + moved[:, 2 * width:]
    packed = packed.reshape(owner_count, CAP, width)
    received = lax.all_to_all(packed, ("depth", "plane"), 0, 0, tiled=True)
    received = received.reshape(owner_count * CAP, vec_count + 1)
    target = received[:, vec_count].astype(jnp.int32)
    choose = (target[:, None] == jnp.arange(PATCH_DEV, dtype=jnp.int32)[None, :]).astype(jnp.float32)
    owned = jnp.einsum(
        "sv,sp->vp", received[:, :vec_count], choose, precision=lax.Precision.HIGHEST,
        preferred_element_type=jnp.float32,
    )
    return (precond[None], owned)


def solution(mesh):
    return jax.shard_map(
        shards,
        mesh=mesh,
        in_specs=(
            P("depth", None, None, "plane"),
            P("depth", None, "plane"),
            P("depth", "plane"),
            P("depth", "plane", None, None, None),
            P("depth", "plane", None),
            P("depth", "plane"),
        ),
        out_specs=(P("depth", None, None, "plane"), P(None, ("depth", "plane"))),
        check_vma=False,
    )
```

```python
import jax
import jax.numpy as jnp
from jax import lax
from jax.sharding import PartitionSpec as P

PATCH_DEV = 128
CAP = 32


def passed_along(value, axis, steps):
    count = lax.axis_size(axis)
    moved = lax.ppermute(value, axis, [(source, (source + steps) % count) for source in range(count)])
    target = lax.axis_index(axis) - steps
    keep = (target >= 0) & (target < count)
    return jnp.where(keep, moved, jnp.zeros_like(moved))


def shards(toar, pml_coeff, coupling, inverse, pattern, patch_map):
    toar_local = toar[0]
    coeff = pml_coeff[0]
    coupler = coupling[0]
    factor = inverse[0]
    pattern_flat = pattern[0].reshape(-1)
    block_rows = factor.shape[0]
    block_cells = factor.shape[2]
    depth_count = lax.axis_size("depth")
    plane_count = lax.axis_size("plane")
    vec_count = toar_local.shape[0]
    toar_f32 = toar_local.astype(jnp.float32)
    real_part = coeff[0] * toar_f32[:, 0] - coeff[1] * toar_f32[:, 1]
    imag_part = coeff[0] * toar_f32[:, 1] + coeff[1] * toar_f32[:, 0]
    source = jnp.stack([real_part, imag_part], axis=1)

    def apply_layer(incoming):
        local_blocks = incoming.reshape(vec_count, 2, block_rows, block_cells).transpose(2, 0, 1, 3)
        local_blocks = local_blocks.reshape(block_rows, vec_count, 2 * block_cells)
        copies = jnp.broadcast_to(local_blocks[None], (plane_count,) + local_blocks.shape)
        gathered = lax.all_to_all(copies, "plane", 0, 0, tiled=True)
        gathered = gathered.reshape(plane_count * block_rows, vec_count, 2 * block_cells)
        chosen = jnp.take(gathered, pattern_flat, axis=0, mode="clip")
        chosen = chosen.reshape(block_rows, -1, vec_count, 2 * block_cells)
        x_re = chosen[..., :block_cells]
        x_im = chosen[..., block_cells:]
        expanded = jnp.stack(
            [jnp.concatenate([x_re, -x_im], axis=-1), jnp.concatenate([x_im, x_re], axis=-1)],
            axis=3,
        )
        out = jnp.einsum(
            "rkic,rkvwc->vwri", factor, expanded, preferred_element_type=jnp.float32
        )
        return out.reshape(vec_count, 2, block_rows * block_cells)

    def down_turn(turn_index, current):
        arrived = passed_along(current, "depth", 1)
        down_in = (source + coupler * arrived.astype(jnp.float32)).astype(jnp.bfloat16)
        return apply_layer(down_in).astype(jnp.bfloat16)

    first = apply_layer(source.astype(jnp.bfloat16)).astype(jnp.bfloat16)
    swept = lax.fori_loop(0, depth_count - 1, down_turn, first)

    def up_turn(turn_index, current):
        outgoing = (coupler * current.astype(jnp.float32)).astype(jnp.bfloat16)
        arrived = passed_along(outgoing, "depth", -1)
        return (swept.astype(jnp.float32) + apply_layer(arrived)).astype(jnp.bfloat16)

    precond = lax.fori_loop(0, depth_count - 1, up_turn, swept)
    product = precond.astype(jnp.float32) * toar_f32
    contrib = product[:, 0] + product[:, 1]

    cell_patch = patch_map[0]
    cell_count = cell_patch.shape[0]
    owner_count = depth_count * plane_count
    owner = cell_patch // PATCH_DEV
    hits = (owner[:, None] == jnp.arange(owner_count, dtype=owner.dtype)[None, :]).astype(jnp.bfloat16)
    cells = jnp.arange(cell_count, dtype=jnp.int32)
    lower = (cells[:, None] >= cells[None, :]).astype(jnp.bfloat16)
    running = jnp.dot(lower, hits, preferred_element_type=jnp.float32)
    rank = jnp.sum(running * hits.astype(jnp.float32), axis=1).astype(jnp.int32) - 1
    slot = owner * CAP + rank
    placed = (slot[:, None] == jnp.arange(owner_count * CAP, dtype=jnp.int32)[None, :]).astype(jnp.bfloat16)
    local_patch = (cell_patch % PATCH_DEV).astype(jnp.float32)
    rows = jnp.concatenate([contrib.T, local_patch[:, None]], axis=1)
    high = lax.reduce_precision(rows, exponent_bits=8, mantissa_bits=7)
    rest = rows - high
    middle = lax.reduce_precision(rest, exponent_bits=8, mantissa_bits=7)
    low = rest - middle
    parts = jnp.concatenate([high, middle, low], axis=1).astype(jnp.bfloat16)
    moved = jnp.einsum("cs,cq->sq", placed, parts, preferred_element_type=jnp.float32)
    width = vec_count + 1
    packed = (moved[:, :width] + moved[:, width:2 * width]) + moved[:, 2 * width:]
    packed = packed.reshape(owner_count, CAP, width)
    received = lax.all_to_all(packed, ("depth", "plane"), 0, 0, tiled=True)
    received = received.reshape(owner_count * CAP, vec_count + 1)
    target = received[:, vec_count].astype(jnp.int32)
    choose = (target[:, None] == jnp.arange(PATCH_DEV, dtype=jnp.int32)[None, :]).astype(jnp.float32)
    owned = jnp.einsum(
        "sv,sp->vp", received[:, :vec_count], choose, precision=lax.Precision.HIGHEST,
        preferred_element_type=jnp.float32,
    )
    return (precond[None], owned)


def solution(mesh):
    return jax.shard_map(
        shards,
        mesh=mesh,
        in_specs=(
            P("depth", None, None, "plane"),
            P("depth", None, "plane"),
            P("depth", "plane"),
            P("depth", "plane", None, None, None),
            P("depth", "plane", None),
            P("depth", "plane"),
        ),
        out_specs=(P("depth", None, None, "plane"), P(None, ("depth", "plane"))),
        check_vma=False,
    )
```

```python
import jax
import jax.numpy as jnp
from jax import lax
from jax.sharding import PartitionSpec as P

PATCH_DEV = 128
CAP = 32


def passed_along(value, axis, steps):
    count = lax.axis_size(axis)
    moved = lax.ppermute(value, axis, [(source, (source + steps) % count) for source in range(count)])
    target = lax.axis_index(axis) - steps
    keep = (target >= 0) & (target < count)
    return jnp.where(keep, moved, jnp.zeros_like(moved))


def shards(toar, pml_coeff, coupling, inverse, pattern, patch_map):
    toar_local = toar[0]
    coeff = pml_coeff[0]
    coupler = coupling[0]
    factor = inverse[0]
    pattern_flat = pattern[0].reshape(-1)
    block_rows = factor.shape[0]
    block_cells = factor.shape[2]
    depth_count = lax.axis_size("depth")
    plane_count = lax.axis_size("plane")
    vec_count = toar_local.shape[0]
    toar_f32 = toar_local.astype(jnp.float32)
    real_part = coeff[0] * toar_f32[:, 0] - coeff[1] * toar_f32[:, 1]
    imag_part = coeff[0] * toar_f32[:, 1] + coeff[1] * toar_f32[:, 0]
    source = jnp.stack([real_part, imag_part], axis=1)

    def apply_layer(incoming):
        local_blocks = incoming.reshape(vec_count, 2, block_rows, block_cells).transpose(2, 0, 1, 3)
        local_blocks = local_blocks.reshape(block_rows, vec_count, 2 * block_cells)
        copies = jnp.broadcast_to(local_blocks[None], (plane_count,) + local_blocks.shape)
        gathered = lax.all_to_all(copies, "plane", 0, 0, tiled=True)
        gathered = gathered.reshape(plane_count * block_rows, vec_count, 2 * block_cells)
        chosen = jnp.take(gathered, pattern_flat, axis=0, mode="clip")
        chosen = chosen.reshape(block_rows, -1, vec_count, 2 * block_cells)
        x_re = chosen[..., :block_cells]
        x_im = chosen[..., block_cells:]
        expanded = jnp.stack(
            [jnp.concatenate([x_re, -x_im], axis=-1), jnp.concatenate([x_im, x_re], axis=-1)],
            axis=3,
        )
        out = jnp.einsum(
            "rkic,rkvwc->vwri", factor, expanded, preferred_element_type=jnp.float32
        )
        return out.reshape(vec_count, 2, block_rows * block_cells)

    def down_turn(turn_index, current):
        arrived = passed_along(current, "depth", 1)
        down_in = (source + coupler * arrived.astype(jnp.float32)).astype(jnp.bfloat16)
        return apply_layer(down_in).astype(jnp.bfloat16)

    swept = apply_layer(source.astype(jnp.bfloat16)).astype(jnp.bfloat16)
    for turn_index in range(depth_count - 1):
        swept = down_turn(turn_index, swept)

    def up_turn(turn_index, current):
        outgoing = (coupler * current.astype(jnp.float32)).astype(jnp.bfloat16)
        arrived = passed_along(outgoing, "depth", -1)
        return (swept.astype(jnp.float32) + apply_layer(arrived)).astype(jnp.bfloat16)

    precond = swept
    for turn_index in range(depth_count - 1):
        precond = up_turn(turn_index, precond)
    cell_patch = patch_map[0]
    cell_count = cell_patch.shape[0]
    owner_count = depth_count * plane_count
    owner = cell_patch // PATCH_DEV
    hits = (owner[:, None] == jnp.arange(owner_count, dtype=owner.dtype)[None, :]).astype(jnp.bfloat16)
    cells = jnp.arange(cell_count, dtype=jnp.int32)
    lower = (cells[:, None] >= cells[None, :]).astype(jnp.bfloat16)
    running = jnp.dot(lower, hits, preferred_element_type=jnp.float32)
    rank = jnp.sum(running * hits.astype(jnp.float32), axis=1).astype(jnp.int32) - 1
    slot = owner * CAP + rank
    placed = (slot[:, None] == jnp.arange(owner_count * CAP, dtype=jnp.int32)[None, :]).astype(jnp.bfloat16)
    local_patch = (cell_patch % PATCH_DEV).astype(jnp.bfloat16)
    toar_rows = jnp.concatenate([toar_local.reshape(-1, cell_count).T, local_patch[:, None]], axis=1)
    toar_moved = jnp.einsum("cs,cq->sq", placed, toar_rows, preferred_element_type=jnp.float32)
    precond_rows = precond.reshape(-1, cell_count).T
    precond_moved = jnp.einsum("cs,cq->sq", placed, precond_rows, preferred_element_type=jnp.float32)
    slots = owner_count * CAP
    product = precond_moved.reshape(slots, vec_count, 2) * toar_moved[:, :-1].reshape(slots, vec_count, 2)
    contrib = product[..., 0] + product[..., 1]
    packed = jnp.concatenate([contrib, toar_moved[:, -1:]], axis=1)
    width = vec_count + 1
    packed = packed.reshape(owner_count, CAP, width)
    received = lax.all_to_all(packed, ("depth", "plane"), 0, 0, tiled=True)
    received = received.reshape(owner_count * CAP, vec_count + 1)
    target = received[:, vec_count].astype(jnp.int32)
    choose = (target[:, None] == jnp.arange(PATCH_DEV, dtype=jnp.int32)[None, :]).astype(jnp.float32)
    owned = jnp.einsum(
        "sv,sp->vp", received[:, :vec_count], choose, precision=lax.Precision.HIGHEST,
        preferred_element_type=jnp.float32,
    )
    return (precond[None], owned)


def solution(mesh):
    return jax.shard_map(
        shards,
        mesh=mesh,
        in_specs=(
            P("depth", None, None, "plane"),
            P("depth", None, "plane"),
            P("depth", "plane"),
            P("depth", "plane", None, None, None),
            P("depth", "plane", None),
            P("depth", "plane"),
        ),
        out_specs=(P("depth", None, None, "plane"), P(None, ("depth", "plane"))),
        check_vma=False,
    )
```

```python
import jax
import jax.numpy as jnp
from jax import lax
from jax.sharding import PartitionSpec as P

PATCH_DEV = 128
CAP = 32


def passed_along(value, axis, steps):
    count = lax.axis_size(axis)
    moved = lax.ppermute(value, axis, [(source, (source + steps) % count) for source in range(count)])
    target = lax.axis_index(axis) - steps
    keep = (target >= 0) & (target < count)
    return jnp.where(keep, moved, jnp.zeros_like(moved))


def shards(toar, pml_coeff, coupling, inverse, pattern, patch_map):
    toar_local = toar[0]
    coeff = pml_coeff[0]
    coupler = coupling[0]
    factor = inverse[0]
    pattern_flat = pattern[0].reshape(-1)
    block_rows = factor.shape[0]
    block_cells = factor.shape[2]
    depth_count = lax.axis_size("depth")
    plane_count = lax.axis_size("plane")
    vec_count = toar_local.shape[0]
    toar_f32 = toar_local.astype(jnp.float32)
    real_part = coeff[0] * toar_f32[:, 0] - coeff[1] * toar_f32[:, 1]
    imag_part = coeff[0] * toar_f32[:, 1] + coeff[1] * toar_f32[:, 0]
    source = jnp.stack([real_part, imag_part], axis=1)

    cell_patch = patch_map[0]
    cell_count = cell_patch.shape[0]
    owner_count = depth_count * plane_count
    owner = cell_patch // PATCH_DEV
    hits = (owner[:, None] == jnp.arange(owner_count, dtype=owner.dtype)[None, :]).astype(jnp.bfloat16)
    cells = jnp.arange(cell_count, dtype=jnp.int32)
    lower = (cells[:, None] >= cells[None, :]).astype(jnp.bfloat16)
    running = jnp.dot(lower, hits, preferred_element_type=jnp.float32)
    rank = jnp.sum(running * hits.astype(jnp.float32), axis=1).astype(jnp.int32) - 1
    slot = owner * CAP + rank
    placed = (slot[:, None] == jnp.arange(owner_count * CAP, dtype=jnp.int32)[None, :]).astype(jnp.bfloat16)
    source, placed = lax.optimization_barrier((source, placed))

    def apply_layer(incoming):
        local_blocks = incoming.reshape(vec_count, 2, block_rows, block_cells).transpose(2, 0, 1, 3)
        local_blocks = local_blocks.reshape(block_rows, vec_count, 2 * block_cells)
        copies = jnp.broadcast_to(local_blocks[None], (plane_count,) + local_blocks.shape)
        gathered = lax.all_to_all(copies, "plane", 0, 0, tiled=True)
        gathered = gathered.reshape(plane_count * block_rows, vec_count, 2 * block_cells)
        chosen = jnp.take(gathered, pattern_flat, axis=0, mode="clip")
        chosen = chosen.reshape(block_rows, -1, vec_count, 2 * block_cells)
        x_re = chosen[..., :block_cells]
        x_im = chosen[..., block_cells:]
        expanded = jnp.stack(
            [jnp.concatenate([x_re, -x_im], axis=-1), jnp.concatenate([x_im, x_re], axis=-1)],
            axis=3,
        )
        out = jnp.einsum(
            "rkic,rkvwc->vwri", factor, expanded, preferred_element_type=jnp.float32
        )
        return out.reshape(vec_count, 2, block_rows * block_cells)

    def down_turn(turn_index, current):
        arrived = passed_along(current, "depth", 1)
        down_in = (source + coupler * arrived.astype(jnp.float32)).astype(jnp.bfloat16)
        return apply_layer(down_in).astype(jnp.bfloat16)

    swept = apply_layer(source.astype(jnp.bfloat16)).astype(jnp.bfloat16)
    for turn_index in range(depth_count - 1):
        swept = down_turn(turn_index, swept)

    def up_turn(turn_index, current):
        outgoing = (coupler * current.astype(jnp.float32)).astype(jnp.bfloat16)
        arrived = passed_along(outgoing, "depth", -1)
        return (swept.astype(jnp.float32) + apply_layer(arrived)).astype(jnp.bfloat16)

    precond = swept
    for turn_index in range(depth_count - 1):
        precond = up_turn(turn_index, precond)
    product = precond.astype(jnp.float32) * toar_f32
    contrib = product[:, 0] + product[:, 1]

    local_patch = (cell_patch % PATCH_DEV).astype(jnp.float32)
    rows = jnp.concatenate([contrib.T, local_patch[:, None]], axis=1)
    high = lax.reduce_precision(rows, exponent_bits=8, mantissa_bits=7)
    rest = rows - high
    middle = lax.reduce_precision(rest, exponent_bits=8, mantissa_bits=7)
    low = rest - middle
    parts = jnp.concatenate([high, middle, low], axis=1).astype(jnp.bfloat16)
    moved = jnp.einsum("cs,cq->sq", placed, parts, preferred_element_type=jnp.float32)
    width = vec_count + 1
    packed = (moved[:, :width] + moved[:, width:2 * width]) + moved[:, 2 * width:]
    packed = packed.reshape(owner_count, CAP, width)
    received = lax.all_to_all(packed, ("depth", "plane"), 0, 0, tiled=True)
    received = received.reshape(owner_count * CAP, vec_count + 1)
    target = received[:, vec_count].astype(jnp.int32)
    choose = (target[:, None] == jnp.arange(PATCH_DEV, dtype=jnp.int32)[None, :]).astype(jnp.float32)
    owned = jnp.einsum(
        "sv,sp->vp", received[:, :vec_count], choose, precision=lax.Precision.HIGHEST,
        preferred_element_type=jnp.float32,
    )
    return (precond[None], owned)


def solution(mesh):
    return jax.shard_map(
        shards,
        mesh=mesh,
        in_specs=(
            P("depth", None, None, "plane"),
            P("depth", None, "plane"),
            P("depth", "plane"),
            P("depth", "plane", None, None, None),
            P("depth", "plane", None),
            P("depth", "plane"),
        ),
        out_specs=(P("depth", None, None, "plane"), P(None, ("depth", "plane"))),
        check_vma=False,
    )
```

```python
import jax
import jax.numpy as jnp
from jax import lax
from jax.sharding import PartitionSpec as P

PATCH_DEV = 128
CAP = 32


def passed_along(value, axis, steps):
    count = lax.axis_size(axis)
    return lax.ppermute(value, axis, [(source, (source + steps) % count) for source in range(count)])


def shards(toar, pml_coeff, coupling, inverse, pattern, patch_map):
    toar_local = toar[0]
    coeff = pml_coeff[0]
    coupler = coupling[0]
    factor = inverse[0]
    pattern_flat = pattern[0].reshape(-1)
    block_rows = factor.shape[0]
    block_cells = factor.shape[2]
    depth_count = lax.axis_size("depth")
    plane_count = lax.axis_size("plane")
    vec_count = toar_local.shape[0]
    toar_f32 = toar_local.astype(jnp.float32)
    real_part = coeff[0] * toar_f32[:, 0] - coeff[1] * toar_f32[:, 1]
    imag_part = coeff[0] * toar_f32[:, 1] + coeff[1] * toar_f32[:, 0]
    source = jnp.stack([real_part, imag_part], axis=1)

    def apply_layer(incoming):
        local_blocks = incoming.reshape(vec_count, 2, block_rows, block_cells).transpose(2, 0, 1, 3)
        local_blocks = local_blocks.reshape(block_rows, vec_count, 2 * block_cells)
        copies = jnp.broadcast_to(local_blocks[None], (plane_count,) + local_blocks.shape)
        gathered = lax.all_to_all(copies, "plane", 0, 0, tiled=True)
        gathered = gathered.reshape(plane_count * block_rows, vec_count, 2 * block_cells)
        chosen = jnp.take(gathered, pattern_flat, axis=0, mode="clip")
        chosen = chosen.reshape(block_rows, -1, vec_count, 2 * block_cells)
        x_re = chosen[..., :block_cells]
        x_im = chosen[..., block_cells:]
        expanded = jnp.stack(
            [jnp.concatenate([x_re, -x_im], axis=-1), jnp.concatenate([x_im, x_re], axis=-1)],
            axis=3,
        )
        out = jnp.einsum(
            "rkic,rkvwc->vwri", factor, expanded, preferred_element_type=jnp.float32
        )
        return out.reshape(vec_count, 2, block_rows * block_cells)

    layer = lax.axis_index("depth")
    coupler_edge = jnp.where(layer > 0, coupler, jnp.zeros_like(coupler))

    def down_turn(turn_index, current):
        arrived = passed_along(current, "depth", 1)
        down_in = (source + coupler_edge * arrived.astype(jnp.float32)).astype(jnp.bfloat16)
        return apply_layer(down_in).astype(jnp.bfloat16)

    swept = apply_layer(source.astype(jnp.bfloat16)).astype(jnp.bfloat16)
    for turn_index in range(depth_count - 1):
        swept = down_turn(turn_index, swept)

    def up_turn(turn_index, current):
        outgoing = (coupler_edge * current.astype(jnp.float32)).astype(jnp.bfloat16)
        arrived = passed_along(outgoing, "depth", -1)
        return (swept.astype(jnp.float32) + apply_layer(arrived)).astype(jnp.bfloat16)

    precond = swept
    for turn_index in range(depth_count - 1):
        precond = up_turn(turn_index, precond)
    product = precond.astype(jnp.float32) * toar_f32
    contrib = product[:, 0] + product[:, 1]

    cell_patch = patch_map[0]
    cell_count = cell_patch.shape[0]
    owner_count = depth_count * plane_count
    owner = cell_patch // PATCH_DEV
    hits = (owner[:, None] == jnp.arange(owner_count, dtype=owner.dtype)[None, :]).astype(jnp.bfloat16)
    cells = jnp.arange(cell_count, dtype=jnp.int32)
    lower = (cells[:, None] >= cells[None, :]).astype(jnp.bfloat16)
    running = jnp.dot(lower, hits, preferred_element_type=jnp.float32)
    rank = jnp.sum(running * hits.astype(jnp.float32), axis=1).astype(jnp.int32) - 1
    slot = owner * CAP + rank
    placed = (slot[:, None] == jnp.arange(owner_count * CAP, dtype=jnp.int32)[None, :]).astype(jnp.bfloat16)
    local_patch = (cell_patch % PATCH_DEV).astype(jnp.float32)
    rows = jnp.concatenate([contrib.T, local_patch[:, None]], axis=1)
    high = lax.reduce_precision(rows, exponent_bits=8, mantissa_bits=7)
    rest = rows - high
    middle = lax.reduce_precision(rest, exponent_bits=8, mantissa_bits=7)
    low = rest - middle
    parts = jnp.concatenate([high, middle, low], axis=1).astype(jnp.bfloat16)
    moved = jnp.einsum("cs,cq->sq", placed, parts, preferred_element_type=jnp.float32)
    width = vec_count + 1
    packed = (moved[:, :width] + moved[:, width:2 * width]) + moved[:, 2 * width:]
    packed = packed.reshape(owner_count, CAP, width)
    received = lax.all_to_all(packed, ("depth", "plane"), 0, 0, tiled=True)
    received = received.reshape(owner_count * CAP, vec_count + 1)
    target = received[:, vec_count].astype(jnp.int32)
    choose = (target[:, None] == jnp.arange(PATCH_DEV, dtype=jnp.int32)[None, :]).astype(jnp.float32)
    owned = jnp.einsum(
        "sv,sp->vp", received[:, :vec_count], choose, precision=lax.Precision.HIGHEST,
        preferred_element_type=jnp.float32,
    )
    return (precond[None], owned)


def solution(mesh):
    return jax.shard_map(
        shards,
        mesh=mesh,
        in_specs=(
            P("depth", None, None, "plane"),
            P("depth", None, "plane"),
            P("depth", "plane"),
            P("depth", "plane", None, None, None),
            P("depth", "plane", None),
            P("depth", "plane"),
        ),
        out_specs=(P("depth", None, None, "plane"), P(None, ("depth", "plane"))),
        check_vma=False,
    )
```

```python
import jax
import jax.numpy as jnp
from jax import lax
from jax.sharding import PartitionSpec as P

PATCH_DEV = 128
CAP = 32


def passed_along(value, axis, steps):
    count = lax.axis_size(axis)
    return lax.ppermute(value, axis, [(source, (source + steps) % count) for source in range(count)])


def shards(toar, pml_coeff, coupling, inverse, pattern, patch_map):
    toar_local = toar[0]
    coeff = pml_coeff[0]
    coupler = coupling[0]
    factor = inverse[0]
    pattern_flat = pattern[0].reshape(-1)
    block_rows = factor.shape[0]
    block_cells = factor.shape[2]
    depth_count = lax.axis_size("depth")
    plane_count = lax.axis_size("plane")
    vec_count = toar_local.shape[0]
    toar_f32 = toar_local.astype(jnp.float32)
    real_part = coeff[0] * toar_f32[:, 0] - coeff[1] * toar_f32[:, 1]
    imag_part = coeff[0] * toar_f32[:, 1] + coeff[1] * toar_f32[:, 0]
    source = jnp.stack([real_part, imag_part], axis=1)

    def apply_layer(incoming):
        local_blocks = incoming.reshape(vec_count, 2, block_rows, block_cells).transpose(2, 0, 1, 3)
        local_blocks = local_blocks.reshape(block_rows, vec_count, 2 * block_cells)
        copies = jnp.broadcast_to(local_blocks[None], (plane_count,) + local_blocks.shape)
        gathered = lax.all_to_all(copies, "plane", 0, 0, tiled=True)
        gathered = gathered.reshape(plane_count * block_rows, vec_count, 2 * block_cells)
        chosen = jnp.take(gathered, pattern_flat, axis=0, mode="clip")
        chosen = chosen.reshape(block_rows, -1, vec_count, 2 * block_cells)
        x_re = chosen[..., :block_cells]
        x_im = chosen[..., block_cells:]
        expanded = jnp.stack(
            [jnp.concatenate([x_re, -x_im], axis=-1), jnp.concatenate([x_im, x_re], axis=-1)],
            axis=3,
        )
        out = jnp.einsum(
            "rkic,rkvwc->vwri", factor, expanded, preferred_element_type=jnp.float32
        )
        return out.reshape(vec_count, 2, block_rows * block_cells)

    layer = lax.axis_index("depth")
    coupler_edge = jnp.where(layer > 0, coupler, jnp.zeros_like(coupler))

    def down_turn(turn_index, current):
        arrived = passed_along(current, "depth", 1)
        down_in = (source + coupler_edge * arrived.astype(jnp.float32)).astype(jnp.bfloat16)
        return apply_layer(down_in).astype(jnp.bfloat16)

    swept = apply_layer(source.astype(jnp.bfloat16)).astype(jnp.bfloat16)
    for turn_index in range(depth_count - 1):
        swept = down_turn(turn_index, swept)

    def up_turn(turn_index, current):
        outgoing = (coupler_edge * current.astype(jnp.float32)).astype(jnp.bfloat16)
        arrived = passed_along(outgoing, "depth", -1)
        return (swept.astype(jnp.float32) + apply_layer(arrived)).astype(jnp.bfloat16)

    precond = swept
    for turn_index in range(depth_count - 1):
        precond = up_turn(turn_index, precond)
    product = precond.astype(jnp.float32) * toar_f32
    contrib = product[:, 0] + product[:, 1]

    cell_patch = patch_map[0]
    cell_count = cell_patch.shape[0]
    owner_count = depth_count * plane_count
    owner = cell_patch // PATCH_DEV
    hits = (owner[:, None] == jnp.arange(owner_count, dtype=owner.dtype)[None, :]).astype(jnp.bfloat16)
    cells = jnp.arange(cell_count, dtype=jnp.int32)
    lower = (cells[:, None] >= cells[None, :]).astype(jnp.bfloat16)
    running = jnp.dot(lower, hits, preferred_element_type=jnp.float32)
    rank = jnp.sum(running * hits.astype(jnp.float32), axis=1).astype(jnp.int32) - 1
    slot = owner * CAP + rank
    placed = (slot[:, None] == jnp.arange(owner_count * CAP, dtype=jnp.int32)[None, :]).astype(jnp.bfloat16)
    local_patch = (cell_patch % PATCH_DEV).astype(jnp.float32)
    rows = jnp.concatenate([contrib.T, local_patch[:, None]], axis=1)
    high = lax.reduce_precision(rows, exponent_bits=8, mantissa_bits=7)
    rest = rows - high
    middle = lax.reduce_precision(rest, exponent_bits=8, mantissa_bits=7)
    low = rest - middle
    parts = jnp.concatenate([high, middle, low], axis=1).astype(jnp.bfloat16)
    moved = jnp.einsum("cs,cq->sq", placed, parts, preferred_element_type=jnp.float32)
    width = vec_count + 1
    packed = (moved[:, :width] + moved[:, width:2 * width]) + moved[:, 2 * width:]
    packed = packed.reshape(owner_count, CAP, width)
    received = lax.all_to_all(packed, ("depth", "plane"), 0, 0, tiled=True)
    received = received.reshape(owner_count * CAP, vec_count + 1)
    target = received[:, vec_count].astype(jnp.int32)
    choose = (target[:, None] == jnp.arange(PATCH_DEV, dtype=jnp.int32)[None, :]).astype(jnp.bfloat16)
    values = received[:, :vec_count]
    top = lax.reduce_precision(values, exponent_bits=8, mantissa_bits=7)
    remainder = values - top
    mid = lax.reduce_precision(remainder, exponent_bits=8, mantissa_bits=7)
    pieces = jnp.concatenate([top, mid, remainder - mid], axis=1).astype(jnp.bfloat16)
    summed = jnp.einsum("sq,sp->qp", pieces, choose, preferred_element_type=jnp.float32)
    owned = (summed[:vec_count] + summed[vec_count:2 * vec_count]) + summed[2 * vec_count:]
    return (precond[None], owned)


def solution(mesh):
    return jax.shard_map(
        shards,
        mesh=mesh,
        in_specs=(
            P("depth", None, None, "plane"),
            P("depth", None, "plane"),
            P("depth", "plane"),
            P("depth", "plane", None, None, None),
            P("depth", "plane", None),
            P("depth", "plane"),
        ),
        out_specs=(P("depth", None, None, "plane"), P(None, ("depth", "plane"))),
        check_vma=False,
    )
```
